256 devices in a mesh: section: 4 (over x), expert: 64 (over y, z, core).
Axes of the slice: x: 4, y: 4, z: 8, core: 2. Of those that a mesh axis runs over, the one named last changes fastest.
Arguments:
- acts: bfloat16 [4, 2, 4096, 3584], P('section', None, 'expert'), may hold values from -6 to 6
- norm_gain: float32 [4, 3584], P('section'), may hold values from 0.1 to 1.9
- router: bfloat16 [4, 3584, 16], P('section'), may hold values from -0.09375 to 0.09375
- routes: int32 [4, 2, 2, 4096, 1], P('section', None, None, 'expert'), may hold values from 0 to 15; in each aligned block of 64 rows (0 to 63, 64 to 127, ..., all dimensions but the last counted through in order) at most 8 rows name the same one
- w_gate: bfloat16 [4, 64, 3584, 256], P('section', 'expert'), may hold values from -0.09375 to 0.09375
- w_up: bfloat16 [4, 64, 3584, 256], P('section', 'expert'), may hold values from -0.09375 to 0.09375
- w_down: bfloat16 [4, 64, 256, 3584], P('section', 'expert'), may hold values from -0.375 to 0.375
Outputs:
- finished: bfloat16 [4, 2, 4096, 3584], P('section', None, 'expert')
The draws below stay inside these ranges and needn't reach their ends.
Inputs may be any that keep to these rules, and one draw needn't show every extreme that they name: `routes`: within each block of 64 tokens of one device, for each layer, round and micro-batch, no expert is named by more than 8 tokens, a bound that some block reaches.
All inputs are finite; a program needn't handle non-finite values.
Results may differ from the reference program's by a relative error of at most 0.0072.
Values may be sent and summed in bfloat16 or wider, within the bound.
No kernel may reach another device: no remote copies, remote signals or barrier semaphores. Data moves between devices by JAX's collectives and lax.ppermute only.
A program may use at most 128 MiB of HBM per device.

```python
import math
import jax
import jax.numpy as jnp
import numpy as np
from jax import lax

D = 3584
GRP = 4
HID = 256
NEXP = 16
TOK_DEV = 64
MB = 2
ROUNDS = 2
CAP = 8
TOKENS = 4096
N_SECTION = 4
N_EXPERT = 64


def shard_levels(stream_key, dims, split, smallest, high):
    loudness, own = 1.0, jax.random.fold_in(stream_key, 6)
    for dim, shards_of in split:
        heights = jnp.exp(jax.random.uniform(jax.random.fold_in(own, dim), (shards_of,), jnp.float32, smallest / len(split), high / len(split)))
        loudness = loudness * jnp.repeat(heights, dims[dim] // shards_of).reshape([-1 if axis == dim else 1 for axis in range(len(dims))])
    return loudness


def shared_out(own_key, own, number, rows, count, top, most, lean):
    sequence = jax.random.permutation(own_key, count)
    crowded, common = portions_of(count, rows * top, most, lean, True), portions_of(count, rows * top, most, lean, False)
    places = jnp.arange(count)

    def named(lengths, turn):
        used = int((lengths > 0).sum())
        fixed = max(1, used // 4)
        moved = fixed + (places - fixed + turn * (used - fixed)) % max(1, count - fixed)
        return jnp.zeros((count,), jnp.int32).at[sequence[jnp.where(places < fixed, places, moved)]].set(jnp.asarray(lengths, jnp.int32))

    lengths = jnp.where(number % 4 == 0, named(crowded, number // 4), named(common, number - number // 4 - 1))
    mixed = jax.random.permutation(jax.random.fold_in(own, 3), count)
    donor, taker = mixed[0:count // 2 * 2:2], mixed[1:count // 2 * 2:2]
    margin = jnp.minimum(lengths[donor] - 1, most - lengths[taker]) // 2
    margin = jnp.where((donor == sequence[0]) | (taker == sequence[0]) | (lengths[taker] == 0), 0, jnp.maximum(margin, 0))
    moved = jax.random.randint(jax.random.fold_in(own, 4), (count // 2,), 0, 1 << 20) % (margin + 1)
    lengths = lengths.at[donor].add(-moved).at[taker].add(moved)
    members = jnp.searchsorted(jnp.cumsum(lengths), jnp.arange(rows * top), side="right").astype(jnp.int32)
    table = members.reshape(top, rows).T
    table = table[jax.random.permutation(jax.random.fold_in(own, 1), rows)]
    turn = jax.random.randint(jax.random.fold_in(own, 2), (rows, 1), 0, top)
    return jnp.take_along_axis(table, (jnp.arange(top)[None, :] + turn) % top, axis=1)


def portions_of(number_of, total, limit, skew, full):
    weights = [(1 << 20) // math.isqrt(rank ** skew) + 1 for rank in range(1, number_of + 1)]
    largest = limit if full else min(limit, max(-(-total // number_of), total * weights[0] // sum(weights)))
    least = 1 if total - largest >= number_of - 1 else 0
    holding, spare = [largest] + [least] * (number_of - 1), total - largest - least * (number_of - 1)
    while spare > 0:
        candidates = [i for i in range(1, number_of) if holding[i] < largest] or [i for i in range(1, number_of) if holding[i] < limit]
        pool, remaining = sum([weights[i] for i in candidates]), spare
        for i in candidates:
            extra = min(limit - holding[i], max(1, remaining * weights[i] // pool), spare)
            holding[i] = holding[i] + extra
            spare = spare - extra
    return np.array(holding)


def noise(own_key, shape, width, limit, cuts=(), held_as=jnp.bfloat16):
    factor_of = shard_levels(own_key, shape, cuts, -0.22, 0.18) if cuts else 1.0
    array = jax.random.normal(own_key, shape, jnp.float32) * width * factor_of
    return jnp.minimum(jnp.maximum(array, -limit), limit).astype(held_as)


def setup_inputs(seed: int = 0) -> dict:
    splits = jax.random.split(jax.random.key(seed), 8)
    acts = noise(splits[0], (N_SECTION, MB, TOKENS, D), 1.0, 6.0, ((0, 4), (2, 64)))
    norm_gain = jnp.clip(1.0 + 0.18 * jax.random.normal(splits[1], (N_SECTION, D), jnp.float32), 0.1, 1.9)
    router = noise(splits[2], (N_SECTION, D, NEXP), D ** -0.5, 0.09375, ((0, 4),))
    routes_keys = jax.random.split(jax.random.fold_in(splits[3], 1), N_SECTION * ROUNDS * MB * TOKENS // TOK_DEV)
    routes_turns = jax.random.permutation(jax.random.fold_in(splits[3], 3), N_SECTION * ROUNDS * MB * TOKENS // TOK_DEV)
    routes = jax.vmap(lambda own, number: shared_out(jax.random.fold_in(splits[3], 2), own, number, TOK_DEV, NEXP, 1, CAP, 2))(routes_keys, routes_turns).reshape((N_SECTION, ROUNDS, MB, TOKENS, 1))
    w_gate = noise(splits[4], (N_SECTION, N_EXPERT, D, HID), D ** -0.5, 0.09375, ((0, 4), (1, 64)))
    w_up = noise(splits[5], (N_SECTION, N_EXPERT, D, HID), D ** -0.5, 0.09375, ((0, 4), (1, 64)))
    w_down = noise(splits[6], (N_SECTION, N_EXPERT, HID, D), HID ** -0.5, 0.375, ((0, 4), (1, 64)))
    return {"acts": acts, "norm_gain": norm_gain, "router": router, "routes": routes, "w_gate": w_gate, "w_up": w_up, "w_down": w_down}


def run_layer(tokens_in, route_ids, gain_row, router_mat, gate_blocks, up_blocks, down_blocks):
    x_float = tokens_in.astype(jnp.float32)
    mean_sq = lax.optimization_barrier(jnp.mean(x_float * x_float, axis=1, keepdims=True))
    normed = (x_float * lax.rsqrt(mean_sq + 1e-06) * gain_row[None, :]).astype(jnp.bfloat16)
    scores = jnp.dot(normed, router_mat, preferred_element_type=jnp.float32)
    chosen = route_ids[:, 0].astype(jnp.int32)
    onehot = (chosen[:, None] == jnp.arange(NEXP, dtype=jnp.int32)[None, :]).astype(jnp.int32)
    gate_val = jax.nn.sigmoid(lax.optimization_barrier(jnp.sum(scores * onehot.astype(jnp.float32), axis=1)))
    per_block = onehot.reshape(N_EXPERT, TOK_DEV, NEXP)
    slot_of = (lax.optimization_barrier(jnp.sum(jnp.cumsum(per_block, axis=1) * per_block, axis=2)) - 1).reshape(TOKENS).astype(jnp.int32)
    source = jnp.repeat(jnp.arange(N_EXPERT, dtype=jnp.int32), TOK_DEV)
    outbox = jnp.zeros((NEXP, N_EXPERT, CAP, D), jnp.bfloat16).at[chosen, source, slot_of].set(normed)
    gate_sorted = jnp.transpose(gate_blocks.reshape(GRP, NEXP, D, HID), (1, 0, 2, 3))
    up_sorted = jnp.transpose(up_blocks.reshape(GRP, NEXP, D, HID), (1, 0, 2, 3))
    down_sorted = jnp.transpose(down_blocks.reshape(GRP, NEXP, HID, D), (1, 0, 2, 3))

    def expert_out(packed):
        rows_box, gate_mats, up_mats, down_mats = packed
        rows_in = rows_box.reshape(N_EXPERT * CAP, D)
        total = jnp.zeros((N_EXPERT * CAP, D), jnp.float32)
        for block_idx in range(GRP):
            gate_proj = jnp.dot(rows_in, gate_mats[block_idx], preferred_element_type=jnp.float32)
            up_proj = jnp.dot(rows_in, up_mats[block_idx], preferred_element_type=jnp.float32)
            hidden = (jax.nn.silu(gate_proj) * up_proj).astype(jnp.bfloat16)
            partial_out = jnp.dot(hidden, down_mats[block_idx], preferred_element_type=jnp.float32).astype(jnp.bfloat16)
            total = total + partial_out.astype(jnp.float32)
        return total
    combined = lax.map(expert_out, (outbox, gate_sorted, up_sorted, down_sorted))
    combined = combined.reshape(NEXP, N_EXPERT, CAP, D)
    picked = combined[chosen, source, slot_of]
    return (x_float + gate_val[:, None] * picked).astype(jnp.bfloat16)

def reference(acts, norm_gain, router, routes, w_gate, w_up, w_down):
    carried = [[acts[group_idx, micro_idx] for micro_idx in range(MB)] for group_idx in range(N_SECTION)]
    for round_idx in range(ROUNDS):
        for group_idx in range(N_SECTION):
            section_idx = (group_idx + round_idx) % N_SECTION
            for micro_idx in range(MB):
                carried[group_idx][micro_idx] = run_layer(carried[group_idx][micro_idx], routes[section_idx, round_idx, micro_idx], norm_gain[section_idx], router[section_idx], w_gate[section_idx], w_up[section_idx], w_down[section_idx])
    result = jnp.stack([jnp.stack(row_list) for row_list in carried])
    return jnp.roll(result, ROUNDS, axis=0)
```

```python
import jax
import jax.numpy as jnp
from jax import lax
from jax.sharding import Mesh
from jax.sharding import PartitionSpec as P

ROW = ("z", "core")
EXP = ("y", "z", "core")


def passed_along(value, axis, steps):
    count = lax.axis_size(axis)
    pairs = [(source, (source + steps) % count) for source in range(count)]
    return lax.ppermute(value, axis, pairs)


def body(acts, norm_gain, router, routes, w_gate, w_up, w_down):
    experts_here = router.shape[2]
    row_size = lax.axis_size("z") * lax.axis_size("core")
    tok_local = acts.shape[2]
    width = acts.shape[3]
    capacity = 2 * tok_local // experts_here
    gain_row = norm_gain[0]
    router_mat = router[0]
    gate_mat = w_gate[0, 0]
    up_mat = w_up[0, 0]
    down_mat = w_down[0, 0]

    def expert_compute(rows_in):
        gate_proj = jnp.dot(rows_in, gate_mat, preferred_element_type=jnp.float32)
        up_proj = jnp.dot(rows_in, up_mat, preferred_element_type=jnp.float32)
        hidden = (jax.nn.silu(gate_proj) * up_proj).astype(jnp.bfloat16)
        return jnp.dot(hidden, down_mat, preferred_element_type=jnp.float32).astype(jnp.bfloat16)

    def apply_layer(tokens_in, route_ids):
        x_float = tokens_in.astype(jnp.float32)
        mean_sq = jnp.mean(x_float * x_float, axis=1, keepdims=True)
        normed = (x_float * lax.rsqrt(mean_sq + 1e-06) * gain_row[None, :]).astype(jnp.bfloat16)
        scores = jnp.dot(normed, router_mat, preferred_element_type=jnp.float32)
        chosen = route_ids[:, 0]
        onehot = (chosen[:, None] == jnp.arange(experts_here, dtype=jnp.int32)[None, :]).astype(
            jnp.int32
        )
        gate_val = jax.nn.sigmoid(jnp.sum(scores * onehot.astype(jnp.float32), axis=1))
        slot_of = jnp.sum(jnp.cumsum(onehot, axis=0) * onehot, axis=1) - 1
        flat_slot = chosen * capacity + slot_of
        placing = (
            flat_slot[None, :] == jnp.arange(experts_here * capacity, dtype=jnp.int32)[:, None]
        ).astype(jnp.bfloat16)
        outbox = jnp.dot(placing, normed, preferred_element_type=jnp.float32).astype(jnp.bfloat16)
        outbox = outbox.reshape(row_size, capacity, width)
        arrived = lax.all_to_all(outbox, ROW, split_axis=0, concat_axis=0, tiled=True)
        rows = lax.all_gather(arrived, "y", axis=0, tiled=True)
        partial_out = expert_compute(rows.reshape(-1, width))
        summed = lax.psum_scatter(partial_out, "y", scatter_dimension=0, tiled=True)
        back = lax.all_to_all(
            summed.reshape(row_size, capacity, width), ROW, split_axis=0, concat_axis=0, tiled=True
        )
        picked = jnp.dot(
            placing.T, back.reshape(experts_here * capacity, width), preferred_element_type=jnp.float32
        )
        return (x_float + gate_val[:, None] * picked).astype(jnp.bfloat16)

    micro_count = acts.shape[1]
    carried = [acts[0, micro_idx] for micro_idx in range(micro_count)]
    for round_idx in range(routes.shape[1]):
        carried = [
            passed_along(apply_layer(carried[micro_idx], routes[0, round_idx, micro_idx]), "section", 1)
            for micro_idx in range(micro_count)
        ]
    return jnp.stack(carried)[None]


def solution(mesh):
    n_sec, n_exp = mesh.devices.shape
    n_core = 2
    n_y = n_exp // (n_core * 8)
    grid = mesh.devices.reshape(n_sec, n_y, n_exp // (n_y * n_core), n_core)
    fine = Mesh(grid, ("section", "y", "z", "core"))
    in_specs = (
        P("section", None, EXP, None),
        P("section", None),
        P("section", None, None),
        P("section", None, None, EXP, None),
        P("section", EXP, None, None),
        P("section", EXP, None, None),
        P("section", EXP, None, None),
    )
    out_specs = P("section", None, EXP, None)
    return jax.shard_map(body, mesh=fine, in_specs=in_specs, out_specs=out_specs, check_vma=False)
```

```python
import jax
import jax.numpy as jnp
from jax import lax
from jax.sharding import Mesh
from jax.sharding import PartitionSpec as P

ROW = ("z", "core")
EXP = ("y", "z", "core")


def passed_along(value, axis, steps):
    count = lax.axis_size(axis)
    pairs = [(source, (source + steps) % count) for source in range(count)]
    return lax.ppermute(value, axis, pairs)


def body(acts, norm_gain, router, routes, w_gate, w_up, w_down):
    experts_here = router.shape[2]
    row_size = lax.axis_size("z") * lax.axis_size("core")
    tok_local = acts.shape[2]
    width = acts.shape[3]
    capacity = 2 * tok_local // experts_here
    gain_row = norm_gain[0]
    router_mat = router[0]
    gate_mat = w_gate[0, 0]
    up_mat = w_up[0, 0]
    down_mat = w_down[0, 0]

    def expert_compute(rows_in):
        gate_proj = jnp.dot(rows_in, gate_mat, preferred_element_type=jnp.float32)
        up_proj = jnp.dot(rows_in, up_mat, preferred_element_type=jnp.float32)
        hidden = (jax.nn.silu(gate_proj) * up_proj).astype(jnp.bfloat16)
        return jnp.dot(hidden, down_mat, preferred_element_type=jnp.float32).astype(jnp.bfloat16)

    def apply_layer(tokens_in, route_ids):
        x_float = tokens_in.astype(jnp.float32)
        mean_sq = jnp.mean(x_float * x_float, axis=1, keepdims=True)
        normed = (x_float * lax.rsqrt(mean_sq + 1e-06) * gain_row[None, :]).astype(jnp.bfloat16)
        scores = jnp.dot(normed, router_mat, preferred_element_type=jnp.float32)
        chosen = route_ids[:, 0]
        onehot = (chosen[:, None] == jnp.arange(experts_here, dtype=jnp.int32)[None, :]).astype(
            jnp.int32
        )
        gate_val = jax.nn.sigmoid(jnp.sum(scores * onehot.astype(jnp.float32), axis=1))
        slot_of = jnp.sum(jnp.cumsum(onehot, axis=0) * onehot, axis=1) - 1
        flat_slot = chosen * capacity + slot_of
        placing = (
            flat_slot[None, :] == jnp.arange(experts_here * capacity, dtype=jnp.int32)[:, None]
        ).astype(jnp.bfloat16)
        outbox = jnp.dot(placing, normed, preferred_element_type=jnp.float32).astype(jnp.bfloat16)
        outbox = outbox.reshape(row_size, capacity, width)
        arrived = lax.all_to_all(outbox, ROW, split_axis=0, concat_axis=0, tiled=True)
        own = arrived.reshape(-1, width)
        half = own.shape[0] // 2
        from_below = passed_along(own, "y", 1)
        from_above = passed_along(own, "y", -1)
        far_low = passed_along(from_below[:half], "y", 1)
        far_high = passed_along(from_above[half:], "y", -1)
        rows = jnp.concatenate([own, from_below, from_above, far_low, far_high], axis=0)
        partial_out = expert_compute(rows)
        q_own, q_below, q_above, q_far_low, q_far_high = jnp.split(
            partial_out, [own.shape[0], 2 * own.shape[0], 3 * own.shape[0], 3 * own.shape[0] + half]
        )
        back_below = passed_along(q_far_low, "y", -1)
        back_above = passed_along(q_far_high, "y", 1)
        direct_below = passed_along(q_below[half:], "y", -1)
        direct_above = passed_along(q_above[:half], "y", 1)
        relay_below = (q_below[:half].astype(jnp.float32) + back_below.astype(jnp.float32)).astype(
            jnp.bfloat16
        )
        relay_above = (q_above[half:].astype(jnp.float32) + back_above.astype(jnp.float32)).astype(
            jnp.bfloat16
        )
        late_below = passed_along(relay_below, "y", -1)
        late_above = passed_along(relay_above, "y", 1)
        lower = (
            q_own[:half].astype(jnp.float32)
            + direct_above.astype(jnp.float32)
            + late_below.astype(jnp.float32)
        )
        upper = (
            q_own[half:].astype(jnp.float32)
            + direct_below.astype(jnp.float32)
            + late_above.astype(jnp.float32)
        )
        summed = jnp.concatenate([lower, upper], axis=0).astype(jnp.bfloat16)
        back = lax.all_to_all(
            summed.reshape(row_size, capacity, width), ROW, split_axis=0, concat_axis=0, tiled=True
        )
        picked = jnp.dot(
            placing.T, back.reshape(experts_here * capacity, width), preferred_element_type=jnp.float32
        )
        return (x_float + gate_val[:, None] * picked).astype(jnp.bfloat16)

    micro_count = acts.shape[1]
    carried = [acts[0, micro_idx] for micro_idx in range(micro_count)]
    for round_idx in range(routes.shape[1]):
        carried = [
            passed_along(apply_layer(carried[micro_idx], routes[0, round_idx, micro_idx]), "section", 1)
            for micro_idx in range(micro_count)
        ]
    return jnp.stack(carried)[None]


def solution(mesh):
    n_sec, n_exp = mesh.devices.shape
    n_core = 2
    n_y = n_exp // (n_core * 8)
    grid = mesh.devices.reshape(n_sec, n_y, n_exp // (n_y * n_core), n_core)
    fine = Mesh(grid, ("section", "y", "z", "core"))
    in_specs = (
        P("section", None, EXP, None),
        P("section", None),
        P("section", None, None),
        P("section", None, None, EXP, None),
        P("section", EXP, None, None),
        P("section", EXP, None, None),
        P("section", EXP, None, None),
    )
    out_specs = P("section", None, EXP, None)
    return jax.shard_map(body, mesh=fine, in_specs=in_specs, out_specs=out_specs, check_vma=False)
```

```python
import jax
import jax.numpy as jnp
from jax import lax
from jax.sharding import Mesh
from jax.sharding import PartitionSpec as P

ROW = ("z", "core")
EXP = ("y", "z", "core")


def passed_along(value, axis, steps):
    count = lax.axis_size(axis)
    pairs = [(source, (source + steps) % count) for source in range(count)]
    return lax.ppermute(value, axis, pairs)


def body(acts, norm_gain, router, routes, w_gate, w_up, w_down):
    experts_here = router.shape[2]
    row_size = lax.axis_size("z") * lax.axis_size("core")
    tok_local = acts.shape[2]
    width = acts.shape[3]
    capacity = 2 * tok_local // experts_here
    gain_row = norm_gain[0]
    router_mat = router[0]
    gate_mat = w_gate[0, 0]
    up_mat = w_up[0, 0]
    down_mat = w_down[0, 0]

    def expert_compute(rows_in):
        gate_proj = jnp.dot(rows_in, gate_mat, preferred_element_type=jnp.float32)
        up_proj = jnp.dot(rows_in, up_mat, preferred_element_type=jnp.float32)
        hidden = (jax.nn.silu(gate_proj) * up_proj).astype(jnp.bfloat16)
        return jnp.dot(hidden, down_mat, preferred_element_type=jnp.float32).astype(jnp.bfloat16)

    def prepare(tokens_in, route_ids):
        x_float = tokens_in.astype(jnp.float32)
        mean_sq = jnp.mean(x_float * x_float, axis=1, keepdims=True)
        normed = (x_float * lax.rsqrt(mean_sq + 1e-06) * gain_row[None, :]).astype(jnp.bfloat16)
        scores = jnp.dot(normed, router_mat, preferred_element_type=jnp.float32)
        chosen = route_ids[:, 0]
        onehot = (chosen[:, None] == jnp.arange(experts_here, dtype=jnp.int32)[None, :]).astype(
            jnp.int32
        )
        gate_val = jax.nn.sigmoid(jnp.sum(scores * onehot.astype(jnp.float32), axis=1))
        slot_of = jnp.sum(jnp.cumsum(onehot, axis=0) * onehot, axis=1) - 1
        flat_slot = chosen * capacity + slot_of
        placing = (
            flat_slot[None, :] == jnp.arange(experts_here * capacity, dtype=jnp.int32)[:, None]
        ).astype(jnp.bfloat16)
        outbox = jnp.dot(placing, normed, preferred_element_type=jnp.float32).astype(jnp.bfloat16)
        outbox = outbox.reshape(row_size, capacity, width)
        return x_float, gate_val, placing, outbox

    def gather_compute(outbox):
        arrived = lax.all_to_all(outbox, ROW, split_axis=0, concat_axis=0, tiled=True)
        own = arrived.reshape(-1, width)
        half = own.shape[0] // 2
        from_below = passed_along(own, "y", 1)
        from_above = passed_along(own, "y", -1)
        far_low = passed_along(from_below[:half], "y", 1)
        far_high = passed_along(from_above[half:], "y", -1)
        rows = jnp.concatenate([own, from_below, from_above, far_low, far_high], axis=0)
        return expert_compute(rows)

    def scatter_back(partial_out, x_float, gate_val, placing):
        half = partial_out.shape[0] // 8
        q_own, q_below, q_above, q_far_low, q_far_high = jnp.split(
            partial_out, [2 * half, 4 * half, 6 * half, 7 * half]
        )
        back_below = passed_along(q_far_low, "y", -1)
        back_above = passed_along(q_far_high, "y", 1)
        direct_below = passed_along(q_below[half:], "y", -1)
        direct_above = passed_along(q_above[:half], "y", 1)
        relay_below = (q_below[:half].astype(jnp.float32) + back_below.astype(jnp.float32)).astype(
            jnp.bfloat16
        )
        relay_above = (q_above[half:].astype(jnp.float32) + back_above.astype(jnp.float32)).astype(
            jnp.bfloat16
        )
        late_below = passed_along(relay_below, "y", -1)
        late_above = passed_along(relay_above, "y", 1)
        lower = (
            q_own[:half].astype(jnp.float32)
            + direct_above.astype(jnp.float32)
            + late_below.astype(jnp.float32)
        )
        upper = (
            q_own[half:].astype(jnp.float32)
            + direct_below.astype(jnp.float32)
            + late_above.astype(jnp.float32)
        )
        summed = jnp.concatenate([lower, upper], axis=0).astype(jnp.bfloat16)
        back = lax.all_to_all(
            summed.reshape(row_size, capacity, width), ROW, split_axis=0, concat_axis=0, tiled=True
        )
        picked = jnp.dot(
            placing.T, back.reshape(experts_here * capacity, width), preferred_element_type=jnp.float32
        )
        return (x_float + gate_val[:, None] * picked).astype(jnp.bfloat16)

    micro_count = acts.shape[1]
    carried = [acts[0, micro_idx] for micro_idx in range(micro_count)]
    for round_idx in range(routes.shape[1]):
        updated = []
        ahead = None
        for micro_idx in range(micro_count):
            x_float, gate_val, placing, outbox = prepare(carried[micro_idx], routes[0, round_idx, micro_idx])
            if ahead is not None:
                outbox, ahead_out = lax.optimization_barrier((outbox, ahead[0]))
                updated.append(scatter_back(ahead_out, *ahead[1:]))
            ahead = (gather_compute(outbox), x_float, gate_val, placing)
        updated.append(scatter_back(*ahead))
        carried = [passed_along(value, "section", 1) for value in updated]
    return jnp.stack(carried)[None]


def solution(mesh):
    n_sec, n_exp = mesh.devices.shape
    n_core = 2
    n_y = n_exp // (n_core * 8)
    grid = mesh.devices.reshape(n_sec, n_y, n_exp // (n_y * n_core), n_core)
    fine = Mesh(grid, ("section", "y", "z", "core"))
    in_specs = (
        P("section", None, EXP, None),
        P("section", None),
        P("section", None, None),
        P("section", None, None, EXP, None),
        P("section", EXP, None, None),
        P("section", EXP, None, None),
        P("section", EXP, None, None),
    )
    out_specs = P("section", None, EXP, None)
    return jax.shard_map(body, mesh=fine, in_specs=in_specs, out_specs=out_specs, check_vma=False)
```

```python
import jax
import jax.numpy as jnp
from jax import lax
from jax.sharding import Mesh
from jax.sharding import PartitionSpec as P

ROW = ("z", "core")
EXP = ("y", "z", "core")


def passed_along(value, axis, steps):
    count = lax.axis_size(axis)
    pairs = [(source, (source + steps) % count) for source in range(count)]
    return lax.ppermute(value, axis, pairs)


def gathered_blocks(block, axis):
    from_below = passed_along(block, "y", 1)
    from_above = passed_along(block, "y", -1)
    far_low = passed_along(jnp.split(from_below, 2, axis=axis)[0], "y", 1)
    far_high = passed_along(jnp.split(from_above, 2, axis=axis)[1], "y", -1)
    return [block, from_below, from_above, jnp.concatenate([far_low, far_high], axis=axis)]


def body(acts, norm_gain, router, routes, w_gate, w_up, w_down):
    experts_here = router.shape[2]
    row_size = lax.axis_size("z") * lax.axis_size("core")
    tok_local = acts.shape[2]
    width = acts.shape[3]
    capacity = 2 * tok_local // experts_here
    gain_row = norm_gain[0]
    router_mat = router[0]
    gate_mats = gathered_blocks(w_gate[0, 0], 0)
    up_mats = gathered_blocks(w_up[0, 0], 0)
    down_mats = gathered_blocks(w_down[0, 0], 0)

    def expert_compute(rows_in):
        total = None
        for gate_mat, up_mat, down_mat in zip(gate_mats, up_mats, down_mats):
            gate_proj = jnp.dot(rows_in, gate_mat, preferred_element_type=jnp.float32)
            up_proj = jnp.dot(rows_in, up_mat, preferred_element_type=jnp.float32)
            hidden = (jax.nn.silu(gate_proj) * up_proj).astype(jnp.bfloat16)
            partial_out = jnp.dot(hidden, down_mat, preferred_element_type=jnp.float32).astype(
                jnp.bfloat16
            )
            term = partial_out.astype(jnp.float32)
            total = term if total is None else total + term
        return total.astype(jnp.bfloat16)

    def apply_layer(tokens_in, route_ids):
        x_float = tokens_in.astype(jnp.float32)
        mean_sq = jnp.mean(x_float * x_float, axis=1, keepdims=True)
        normed = (x_float * lax.rsqrt(mean_sq + 1e-06) * gain_row[None, :]).astype(jnp.bfloat16)
        scores = jnp.dot(normed, router_mat, preferred_element_type=jnp.float32)
        chosen = route_ids[:, 0]
        onehot = (chosen[:, None] == jnp.arange(experts_here, dtype=jnp.int32)[None, :]).astype(
            jnp.int32
        )
        gate_val = jax.nn.sigmoid(jnp.sum(scores * onehot.astype(jnp.float32), axis=1))
        slot_of = jnp.sum(jnp.cumsum(onehot, axis=0) * onehot, axis=1) - 1
        flat_slot = chosen * capacity + slot_of
        placing = (
            flat_slot[None, :] == jnp.arange(experts_here * capacity, dtype=jnp.int32)[:, None]
        ).astype(jnp.bfloat16)
        outbox = jnp.dot(placing, normed, preferred_element_type=jnp.float32).astype(jnp.bfloat16)
        outbox = outbox.reshape(row_size, capacity, width)
        arrived = lax.all_to_all(outbox, ROW, split_axis=0, concat_axis=0, tiled=True)
        summed = expert_compute(arrived.reshape(-1, width))
        back = lax.all_to_all(
            summed.reshape(row_size, capacity, width), ROW, split_axis=0, concat_axis=0, tiled=True
        )
        picked = jnp.dot(
            placing.T, back.reshape(experts_here * capacity, width), preferred_element_type=jnp.float32
        )
        return (x_float + gate_val[:, None] * picked).astype(jnp.bfloat16)

    micro_count = acts.shape[1]
    carried = [acts[0, micro_idx] for micro_idx in range(micro_count)]
    for round_idx in range(routes.shape[1]):
        carried = [
            passed_along(apply_layer(carried[micro_idx], routes[0, round_idx, micro_idx]), "section", 1)
            for micro_idx in range(micro_count)
        ]
    return jnp.stack(carried)[None]


def solution(mesh):
    n_sec, n_exp = mesh.devices.shape
    n_core = 2
    n_y = n_exp // (n_core * 8)
    grid = mesh.devices.reshape(n_sec, n_y, n_exp // (n_y * n_core), n_core)
    fine = Mesh(grid, ("section", "y", "z", "core"))
    in_specs = (
        P("section", None, EXP, None),
        P("section", None),
        P("section", None, None),
        P("section", None, None, EXP, None),
        P("section", EXP, None, None),
        P("section", EXP, None, None),
        P("section", EXP, None, None),
    )
    out_specs = P("section", None, EXP, None)
    return jax.shard_map(body, mesh=fine, in_specs=in_specs, out_specs=out_specs, check_vma=False)
```

```python
import jax
import jax.numpy as jnp
from jax import lax
from jax.sharding import Mesh
from jax.sharding import PartitionSpec as P

ROW = ("z", "core")
EXP = ("y", "z", "core")


def passed_along(value, axis, steps):
    count = lax.axis_size(axis)
    pairs = [(source, (source + steps) % count) for source in range(count)]
    return lax.ppermute(value, axis, pairs)


def neighbour_blocks(block):
    return block, passed_along(block, "y", 1), passed_along(block, "y", -1)


def far_block(from_below, from_above, axis):
    far_low = passed_along(jnp.split(from_below, 2, axis=axis)[0], "y", 1)
    far_high = passed_along(jnp.split(from_above, 2, axis=axis)[1], "y", -1)
    return jnp.concatenate([far_low, far_high], axis=axis)


def body(acts, norm_gain, router, routes, w_gate, w_up, w_down):
    experts_here = router.shape[2]
    row_size = lax.axis_size("z") * lax.axis_size("core")
    tok_local = acts.shape[2]
    width = acts.shape[3]
    capacity = 2 * tok_local // experts_here
    gain_row = norm_gain[0]
    router_mat = router[0]
    near = [neighbour_blocks(w[0, 0]) for w in (w_gate, w_up, w_down)]
    own_w, below_w, above_w = [tuple(mats[k] for mats in near) for k in range(3)]
    far_w = tuple(far_block(mats[1], mats[2], 0) for mats in near)

    def expert_partial(rows_in, mats):
        gate_mat, up_mat, down_mat = mats
        gate_proj = jnp.dot(rows_in, gate_mat, preferred_element_type=jnp.float32)
        up_proj = jnp.dot(rows_in, up_mat, preferred_element_type=jnp.float32)
        hidden = (jax.nn.silu(gate_proj) * up_proj).astype(jnp.bfloat16)
        return jnp.dot(hidden, down_mat, preferred_element_type=jnp.float32).astype(jnp.bfloat16)

    def expert_compute(rows_in, exchange):
        terms = [expert_partial(rows_in, mats) for mats in (own_w, below_w, above_w)]
        if exchange:
            half = rows_in.shape[0] // 2
            from_below = passed_along(rows_in[:half], "y", 1)
            from_above = passed_along(rows_in[half:], "y", -1)
            done_below = passed_along(expert_partial(from_below, above_w), "y", -1)
            done_above = passed_along(expert_partial(from_above, below_w), "y", 1)
            terms.append(jnp.concatenate([done_below, done_above], axis=0))
        else:
            terms.append(expert_partial(rows_in, far_w))
        total = terms[0].astype(jnp.float32)
        for term in terms[1:]:
            total = total + term.astype(jnp.float32)
        return total.astype(jnp.bfloat16)

    def apply_layer(tokens_in, route_ids, exchange):
        x_float = tokens_in.astype(jnp.float32)
        mean_sq = jnp.mean(x_float * x_float, axis=1, keepdims=True)
        normed = (x_float * lax.rsqrt(mean_sq + 1e-06) * gain_row[None, :]).astype(jnp.bfloat16)
        scores = jnp.dot(normed, router_mat, preferred_element_type=jnp.float32)
        chosen = route_ids[:, 0]
        onehot = (chosen[:, None] == jnp.arange(experts_here, dtype=jnp.int32)[None, :]).astype(
            jnp.int32
        )
        gate_val = jax.nn.sigmoid(jnp.sum(scores * onehot.astype(jnp.float32), axis=1))
        slot_of = jnp.sum(jnp.cumsum(onehot, axis=0) * onehot, axis=1) - 1
        flat_slot = chosen * capacity + slot_of
        placing = (
            flat_slot[None, :] == jnp.arange(experts_here * capacity, dtype=jnp.int32)[:, None]
        ).astype(jnp.bfloat16)
        outbox = jnp.dot(placing, normed, preferred_element_type=jnp.float32).astype(jnp.bfloat16)
        outbox = outbox.reshape(row_size, capacity, width)
        arrived = lax.all_to_all(outbox, ROW, split_axis=0, concat_axis=0, tiled=True)
        summed = expert_compute(arrived.reshape(-1, width), exchange)
        back = lax.all_to_all(
            summed.reshape(row_size, capacity, width), ROW, split_axis=0, concat_axis=0, tiled=True
        )
        picked = jnp.dot(
            placing.T, back.reshape(experts_here * capacity, width), preferred_element_type=jnp.float32
        )
        return (x_float + gate_val[:, None] * picked).astype(jnp.bfloat16)

    micro_count = acts.shape[1]
    carried = [acts[0, micro_idx] for micro_idx in range(micro_count)]
    for round_idx in range(routes.shape[1]):
        carried = [
            passed_along(
                apply_layer(carried[micro_idx], routes[0, round_idx, micro_idx], round_idx == 0),
                "section",
                1,
            )
            for micro_idx in range(micro_count)
        ]
    return jnp.stack(carried)[None]


def solution(mesh):
    n_sec, n_exp = mesh.devices.shape
    n_core = 2
    n_y = n_exp // (n_core * 8)
    grid = mesh.devices.reshape(n_sec, n_y, n_exp // (n_y * n_core), n_core)
    fine = Mesh(grid, ("section", "y", "z", "core"))
    in_specs = (
        P("section", None, EXP, None),
        P("section", None),
        P("section", None, None),
        P("section", None, None, EXP, None),
        P("section", EXP, None, None),
        P("section", EXP, None, None),
        P("section", EXP, None, None),
    )
    out_specs = P("section", None, EXP, None)
    return jax.shard_map(body, mesh=fine, in_specs=in_specs, out_specs=out_specs, check_vma=False)
```

```python
import jax
import jax.numpy as jnp
from jax import lax
from jax.sharding import Mesh
from jax.sharding import PartitionSpec as P

ROW = ("z", "core")
EXP = ("y", "z", "core")


def passed_along(value, axis, steps):
    count = lax.axis_size(axis)
    pairs = [(source, (source + steps) % count) for source in range(count)]
    return lax.ppermute(value, axis, pairs)


def gathered_blocks(block, axis):
    from_below = passed_along(block, "y", 1)
    from_above = passed_along(block, "y", -1)
    far_low = passed_along(jnp.split(from_below, 2, axis=axis)[0], "y", 1)
    far_high = passed_along(jnp.split(from_above, 2, axis=axis)[1], "y", -1)
    return [block, from_below, from_above, jnp.concatenate([far_low, far_high], axis=axis)]


def body(acts, norm_gain, router, routes, w_gate, w_up, w_down):
    experts_here = router.shape[2]
    row_size = lax.axis_size("z") * lax.axis_size("core")
    tok_local = acts.shape[2]
    width = acts.shape[3]
    capacity = 2 * tok_local // experts_here
    gain_row = norm_gain[0]
    router_mat = router[0]
    gate_mats = gathered_blocks(w_gate[0, 0], 0)
    up_mats = gathered_blocks(w_up[0, 0], 0)
    down_mats = gathered_blocks(w_down[0, 0], 0)
    hid_total = sum(mat.shape[1] for mat in gate_mats)
    gate_up = jnp.concatenate(gate_mats + up_mats, axis=1)
    down_all = jnp.concatenate(down_mats, axis=0)

    def expert_compute(rows_in):
        both = jnp.dot(rows_in, gate_up, preferred_element_type=jnp.float32)
        hidden = (jax.nn.silu(both[:, :hid_total]) * both[:, hid_total:]).astype(jnp.bfloat16)
        return jnp.dot(hidden, down_all, preferred_element_type=jnp.float32).astype(jnp.bfloat16)

    def apply_layer(tokens_in, route_ids):
        x_float = tokens_in.astype(jnp.float32)
        mean_sq = jnp.mean(x_float * x_float, axis=1, keepdims=True)
        normed = (x_float * lax.rsqrt(mean_sq + 1e-06) * gain_row[None, :]).astype(jnp.bfloat16)
        scores = jnp.dot(normed, router_mat, preferred_element_type=jnp.float32)
        chosen = route_ids[:, 0]
        onehot = (chosen[:, None] == jnp.arange(experts_here, dtype=jnp.int32)[None, :]).astype(
            jnp.int32
        )
        gate_val = jax.nn.sigmoid(jnp.sum(scores * onehot.astype(jnp.float32), axis=1))
        slot_of = jnp.sum(jnp.cumsum(onehot, axis=0) * onehot, axis=1) - 1
        flat_slot = chosen * capacity + slot_of
        placing = (
            flat_slot[None, :] == jnp.arange(experts_here * capacity, dtype=jnp.int32)[:, None]
        ).astype(jnp.bfloat16)
        outbox = jnp.dot(placing, normed, preferred_element_type=jnp.float32).astype(jnp.bfloat16)
        outbox = outbox.reshape(row_size, capacity, width)
        arrived = lax.all_to_all(outbox, ROW, split_axis=0, concat_axis=0, tiled=True)
        summed = expert_compute(arrived.reshape(-1, width))
        back = lax.all_to_all(
            summed.reshape(row_size, capacity, width), ROW, split_axis=0, concat_axis=0, tiled=True
        )
        picked = jnp.dot(
            placing.T, back.reshape(experts_here * capacity, width), preferred_element_type=jnp.float32
        )
        return (x_float + gate_val[:, None] * picked).astype(jnp.bfloat16)

    micro_count = acts.shape[1]
    carried = [acts[0, micro_idx] for micro_idx in range(micro_count)]
    for round_idx in range(routes.shape[1]):
        carried = [
            passed_along(apply_layer(carried[micro_idx], routes[0, round_idx, micro_idx]), "section", 1)
            for micro_idx in range(micro_count)
        ]
    return jnp.stack(carried)[None]


def solution(mesh):
    n_sec, n_exp = mesh.devices.shape
    n_core = 2
    n_y = n_exp // (n_core * 8)
    grid = mesh.devices.reshape(n_sec, n_y, n_exp // (n_y * n_core), n_core)
    fine = Mesh(grid, ("section", "y", "z", "core"))
    in_specs = (
        P("section", None, EXP, None),
        P("section", None),
        P("section", None, None),
        P("section", None, None, EXP, None),
        P("section", EXP, None, None),
        P("section", EXP, None, None),
        P("section", EXP, None, None),
    )
    out_specs = P("section", None, EXP, None)
    return jax.shard_map(body, mesh=fine, in_specs=in_specs, out_specs=out_specs, check_vma=False)
```

```python
import jax
import jax.numpy as jnp
from jax import lax
from jax.sharding import Mesh
from jax.sharding import PartitionSpec as P

ROW = ("z", "core")
EXP = ("y", "z", "core")


def passed_along(value, axis, steps):
    count = lax.axis_size(axis)
    pairs = [(source, (source + steps) % count) for source in range(count)]
    return lax.ppermute(value, axis, pairs)


def gathered_blocks(block, axis):
    from_below = passed_along(block, "y", 1)
    from_above = passed_along(block, "y", -1)
    far_low = passed_along(jnp.split(from_below, 2, axis=axis)[0], "y", 1)
    far_high = passed_along(jnp.split(from_above, 2, axis=axis)[1], "y", -1)
    return [block, from_below, from_above, jnp.concatenate([far_low, far_high], axis=axis)]


def body(acts, norm_gain, router, routes, w_gate, w_up, w_down):
    experts_here = router.shape[2]
    row_size = lax.axis_size("z") * lax.axis_size("core")
    tok_local = acts.shape[2]
    width = acts.shape[3]
    capacity = 2 * tok_local // experts_here
    gain_row = norm_gain[0]
    router_mat = router[0]
    gate_mats = gathered_blocks(w_gate[0, 0], 0)
    up_mats = gathered_blocks(w_up[0, 0], 0)
    down_mats = gathered_blocks(w_down[0, 0], 0)
    hid_total = sum(mat.shape[1] for mat in gate_mats)
    gate_up = jnp.concatenate(gate_mats + up_mats, axis=1)
    down_all = jnp.concatenate(down_mats, axis=0)

    def expert_compute(rows_in):
        both = jnp.dot(rows_in, gate_up, preferred_element_type=jnp.float32)
        hidden = (jax.nn.silu(both[:, :hid_total]) * both[:, hid_total:]).astype(jnp.bfloat16)
        return jnp.dot(hidden, down_all, preferred_element_type=jnp.float32).astype(jnp.bfloat16)

    def prepare(tokens_in, route_ids):
        x_float = tokens_in.astype(jnp.float32)
        mean_sq = jnp.mean(x_float * x_float, axis=1, keepdims=True)
        normed = (x_float * lax.rsqrt(mean_sq + 1e-06) * gain_row[None, :]).astype(jnp.bfloat16)
        scores = jnp.dot(normed, router_mat, preferred_element_type=jnp.float32)
        chosen = route_ids[:, 0]
        onehot = (chosen[:, None] == jnp.arange(experts_here, dtype=jnp.int32)[None, :]).astype(
            jnp.int32
        )
        gate_val = jax.nn.sigmoid(jnp.sum(scores * onehot.astype(jnp.float32), axis=1))
        slot_of = jnp.sum(jnp.cumsum(onehot, axis=0) * onehot, axis=1) - 1
        flat_slot = chosen * capacity + slot_of
        placing = (
            flat_slot[None, :] == jnp.arange(experts_here * capacity, dtype=jnp.int32)[:, None]
        ).astype(jnp.bfloat16)
        outbox = jnp.dot(placing, normed, preferred_element_type=jnp.float32).astype(jnp.bfloat16)
        return x_float, gate_val, placing, outbox.reshape(row_size, capacity, width)

    def finish(arrived, x_float, gate_val, placing):
        summed = expert_compute(arrived.reshape(-1, width))
        back = lax.all_to_all(
            summed.reshape(row_size, capacity, width), ROW, split_axis=0, concat_axis=0, tiled=True
        )
        picked = jnp.dot(
            placing.T, back.reshape(experts_here * capacity, width), preferred_element_type=jnp.float32
        )
        return (x_float + gate_val[:, None] * picked).astype(jnp.bfloat16)

    micro_count = acts.shape[1]
    carried = [acts[0, micro_idx] for micro_idx in range(micro_count)]
    for round_idx in range(routes.shape[1]):
        ready = [prepare(carried[m], routes[0, round_idx, m]) for m in range(micro_count)]
        if round_idx == 0:
            stacked = jnp.stack([parts[3] for parts in ready], axis=1)
            together = lax.all_to_all(stacked, ROW, split_axis=0, concat_axis=0, tiled=True)
            arrivals = [together[:, m] for m in range(micro_count)]
        else:
            arrivals = [
                lax.all_to_all(parts[3], ROW, split_axis=0, concat_axis=0, tiled=True)
                for parts in ready
            ]
        carried = [
            passed_along(finish(arrivals[m], *ready[m][:3]), "section", 1)
            for m in range(micro_count)
        ]
    return jnp.stack(carried)[None]


def solution(mesh):
    n_sec, n_exp = mesh.devices.shape
    n_core = 2
    n_y = n_exp // (n_core * 8)
    grid = mesh.devices.reshape(n_sec, n_y, n_exp // (n_y * n_core), n_core)
    fine = Mesh(grid, ("section", "y", "z", "core"))
    in_specs = (
        P("section", None, EXP, None),
        P("section", None),
        P("section", None, None),
        P("section", None, None, EXP, None),
        P("section", EXP, None, None),
        P("section", EXP, None, None),
        P("section", EXP, None, None),
    )
    out_specs = P("section", None, EXP, None)
    return jax.shard_map(body, mesh=fine, in_specs=in_specs, out_specs=out_specs, check_vma=False)
```

```python
import jax
import jax.numpy as jnp
from jax import lax
from jax.sharding import Mesh
from jax.sharding import PartitionSpec as P

ROW = ("z", "core")
EXP = ("y", "z", "core")


def passed_along(value, axis, steps):
    count = lax.axis_size(axis)
    pairs = [(source, (source + steps) % count) for source in range(count)]
    return lax.ppermute(value, axis, pairs)


def gathered_blocks(block, axis):
    from_below = passed_along(block, "y", 1)
    from_above = passed_along(block, "y", -1)
    far_low = passed_along(jnp.split(from_below, 2, axis=axis)[0], "y", 1)
    far_high = passed_along(jnp.split(from_above, 2, axis=axis)[1], "y", -1)
    return [block, from_below, from_above], [far_low, far_high]


def body(acts, norm_gain, router, routes, w_gate, w_up, w_down):
    experts_here = router.shape[2]
    row_size = lax.axis_size("z") * lax.axis_size("core")
    tok_local = acts.shape[2]
    width = acts.shape[3]
    capacity = 2 * tok_local // experts_here
    gain_row = norm_gain[0]
    router_mat = router[0]
    gate_near, gate_far = gathered_blocks(w_gate[0, 0], 1)
    up_near, up_far = gathered_blocks(w_up[0, 0], 1)
    down_near, down_far = gathered_blocks(w_down[0, 0], 0)
    near_hid = sum(mat.shape[1] for mat in gate_near)
    far_hid = sum(mat.shape[1] for mat in gate_far)
    near_gate_up = jnp.concatenate(gate_near + up_near, axis=1)
    near_down = jnp.concatenate(down_near, axis=0)
    far_gate_up = jnp.concatenate(gate_far + up_far, axis=1)
    far_down = jnp.concatenate(down_far, axis=0)

    def expert_part(rows_in, gate_up, down_all, hid):
        both = jnp.dot(rows_in, gate_up, preferred_element_type=jnp.float32)
        hidden = (jax.nn.silu(both[:, :hid]) * both[:, hid:]).astype(jnp.bfloat16)
        return jnp.dot(hidden, down_all, preferred_element_type=jnp.float32)

    def expert_compute(rows_in):
        near = expert_part(rows_in, near_gate_up, near_down, near_hid)
        far = expert_part(rows_in, far_gate_up, far_down, far_hid)
        return (near + far).astype(jnp.bfloat16)

    def prepare(tokens_in, route_ids):
        x_float = tokens_in.astype(jnp.float32)
        mean_sq = jnp.mean(x_float * x_float, axis=1, keepdims=True)
        normed = (x_float * lax.rsqrt(mean_sq + 1e-06) * gain_row[None, :]).astype(jnp.bfloat16)
        scores = jnp.dot(normed, router_mat, preferred_element_type=jnp.float32)
        chosen = route_ids[:, 0]
        onehot = (chosen[:, None] == jnp.arange(experts_here, dtype=jnp.int32)[None, :]).astype(
            jnp.int32
        )
        gate_val = jax.nn.sigmoid(jnp.sum(scores * onehot.astype(jnp.float32), axis=1))
        slot_of = jnp.sum(jnp.cumsum(onehot, axis=0) * onehot, axis=1) - 1
        flat_slot = chosen * capacity + slot_of
        placing = (
            flat_slot[None, :] == jnp.arange(experts_here * capacity, dtype=jnp.int32)[:, None]
        ).astype(jnp.bfloat16)
        outbox = jnp.dot(placing, normed, preferred_element_type=jnp.float32).astype(jnp.bfloat16)
        return x_float, gate_val, placing, outbox.reshape(row_size, capacity, width)

    def finish(arrived, x_float, gate_val, placing):
        summed = expert_compute(arrived.reshape(-1, width))
        back = lax.all_to_all(
            summed.reshape(row_size, capacity, width), ROW, split_axis=0, concat_axis=0, tiled=True
        )
        picked = jnp.dot(
            placing.T, back.reshape(experts_here * capacity, width), preferred_element_type=jnp.float32
        )
        return (x_float + gate_val[:, None] * picked).astype(jnp.bfloat16)

    micro_count = acts.shape[1]
    carried = [acts[0, micro_idx] for micro_idx in range(micro_count)]
    for round_idx in range(routes.shape[1]):
        ready = [prepare(carried[m], routes[0, round_idx, m]) for m in range(micro_count)]
        if round_idx == 0:
            stacked = jnp.stack([parts[3] for parts in ready], axis=1)
            together = lax.all_to_all(stacked, ROW, split_axis=0, concat_axis=0, tiled=True)
            arrivals = [together[:, m] for m in range(micro_count)]
        else:
            arrivals = [
                lax.all_to_all(parts[3], ROW, split_axis=0, concat_axis=0, tiled=True)
                for parts in ready
            ]
        carried = [
            passed_along(finish(arrivals[m], *ready[m][:3]), "section", 1)
            for m in range(micro_count)
        ]
    return jnp.stack(carried)[None]


def solution(mesh):
    n_sec, n_exp = mesh.devices.shape
    n_core = 2
    n_y = n_exp // (n_core * 8)
    grid = mesh.devices.reshape(n_sec, n_y, n_exp // (n_y * n_core), n_core)
    fine = Mesh(grid, ("section", "y", "z", "core"))
    in_specs = (
        P("section", None, EXP, None),
        P("section", None),
        P("section", None, None),
        P("section", None, None, EXP, None),
        P("section", EXP, None, None),
        P("section", EXP, None, None),
        P("section", EXP, None, None),
    )
    out_specs = P("section", None, EXP, None)
    return jax.shard_map(body, mesh=fine, in_specs=in_specs, out_specs=out_specs, check_vma=False)
```

```python
import jax
import jax.numpy as jnp
from jax import lax
from jax.sharding import Mesh
from jax.sharding import PartitionSpec as P

ROW = ("z", "core")
EXP = ("y", "z", "core")


def passed_along(value, axis, steps):
    count = lax.axis_size(axis)
    pairs = [(source, (source + steps) % count) for source in range(count)]
    return lax.ppermute(value, axis, pairs)


def gathered_blocks(block, axis):
    from_below = passed_along(block, "y", 1)
    from_above = passed_along(block, "y", -1)
    far_low = passed_along(jnp.split(from_below, 2, axis=axis)[0], "y", 1)
    far_high = passed_along(jnp.split(from_above, 2, axis=axis)[1], "y", -1)
    return [block, from_below, from_above], [far_low, far_high]


def body(acts, norm_gain, router, routes, w_gate, w_up, w_down):
    experts_here = router.shape[2]
    row_size = lax.axis_size("z") * lax.axis_size("core")
    tok_local = acts.shape[2]
    width = acts.shape[3]
    capacity = 2 * tok_local // experts_here
    gain_row = norm_gain[0]
    router_mat = router[0]
    gate_near, gate_far = gathered_blocks(w_gate[0, 0], 1)
    up_near, up_far = gathered_blocks(w_up[0, 0], 1)
    down_near, down_far = gathered_blocks(w_down[0, 0], 0)
    near_hid = sum(mat.shape[1] for mat in gate_near)
    far_hid = sum(mat.shape[1] for mat in gate_far)
    near_gate_up = jnp.concatenate(gate_near + up_near, axis=1)
    near_down = jnp.concatenate(down_near, axis=0)
    far_gate_up = jnp.concatenate(gate_far + up_far, axis=1)
    far_down = jnp.concatenate(down_far, axis=0)

    def expert_part(rows_in, gate_up, down_all, hid):
        both = jnp.dot(rows_in, gate_up, preferred_element_type=jnp.float32)
        hidden = (jax.nn.silu(both[:, :hid]) * both[:, hid:]).astype(jnp.bfloat16)
        return jnp.dot(hidden, down_all, preferred_element_type=jnp.float32)

    def expert_compute(rows_in):
        near = expert_part(rows_in, near_gate_up, near_down, near_hid)
        far_gate_up_held, far_down_held, near = lax.optimization_barrier((far_gate_up, far_down, near))
        far = expert_part(rows_in, far_gate_up_held, far_down_held, far_hid)
        return (near + far).astype(jnp.bfloat16)

    def prepare(tokens_in, route_ids):
        x_float = tokens_in.astype(jnp.float32)
        mean_sq = jnp.mean(x_float * x_float, axis=1, keepdims=True)
        normed = (x_float * lax.rsqrt(mean_sq + 1e-06) * gain_row[None, :]).astype(jnp.bfloat16)
        scores = jnp.dot(normed, router_mat, preferred_element_type=jnp.float32)
        chosen = route_ids[:, 0]
        onehot = (chosen[:, None] == jnp.arange(experts_here, dtype=jnp.int32)[None, :]).astype(
            jnp.int32
        )
        gate_val = jax.nn.sigmoid(jnp.sum(scores * onehot.astype(jnp.float32), axis=1))
        slot_of = jnp.sum(jnp.cumsum(onehot, axis=0) * onehot, axis=1) - 1
        flat_slot = chosen * capacity + slot_of
        placing = (
            flat_slot[None, :] == jnp.arange(experts_here * capacity, dtype=jnp.int32)[:, None]
        ).astype(jnp.bfloat16)
        outbox = jnp.dot(placing, normed, preferred_element_type=jnp.float32).astype(jnp.bfloat16)
        return x_float, gate_val, placing, outbox.reshape(row_size, capacity, width)

    def finish(arrived, x_float, gate_val, placing):
        summed = expert_compute(arrived.reshape(-1, width))
        back = lax.all_to_all(
            summed.reshape(row_size, capacity, width), ROW, split_axis=0, concat_axis=0, tiled=True
        )
        picked = jnp.dot(
            placing.T, back.reshape(experts_here * capacity, width), preferred_element_type=jnp.float32
        )
        return (x_float + gate_val[:, None] * picked).astype(jnp.bfloat16)

    micro_count = acts.shape[1]
    carried = [acts[0, micro_idx] for micro_idx in range(micro_count)]
    for round_idx in range(routes.shape[1]):
        ready = [prepare(carried[m], routes[0, round_idx, m]) for m in range(micro_count)]
        if round_idx == 0:
            stacked = jnp.stack([parts[3] for parts in ready], axis=1)
            together = lax.all_to_all(stacked, ROW, split_axis=0, concat_axis=0, tiled=True)
            arrivals = [together[:, m] for m in range(micro_count)]
        else:
            arrivals = [
                lax.all_to_all(parts[3], ROW, split_axis=0, concat_axis=0, tiled=True)
                for parts in ready
            ]
        carried = [
            passed_along(finish(arrivals[m], *ready[m][:3]), "section", 1)
            for m in range(micro_count)
        ]
    return jnp.stack(carried)[None]


def solution(mesh):
    n_sec, n_exp = mesh.devices.shape
    n_core = 2
    n_y = n_exp // (n_core * 8)
    grid = mesh.devices.reshape(n_sec, n_y, n_exp // (n_y * n_core), n_core)
    fine = Mesh(grid, ("section", "y", "z", "core"))
    in_specs = (
        P("section", None, EXP, None),
        P("section", None),
        P("section", None, None),
        P("section", None, None, EXP, None),
        P("section", EXP, None, None),
        P("section", EXP, None, None),
        P("section", EXP, None, None),
    )
    out_specs = P("section", None, EXP, None)
    return jax.shard_map(body, mesh=fine, in_specs=in_specs, out_specs=out_specs, check_vma=False)
```

```python
import jax
import jax.numpy as jnp
from jax import lax
from jax.sharding import Mesh
from jax.sharding import PartitionSpec as P

ROW = ("z", "core")
EXP = ("y", "z", "core")


def passed_along(value, axis, steps):
    count = lax.axis_size(axis)
    pairs = [(source, (source + steps) % count) for source in range(count)]
    return lax.ppermute(value, axis, pairs)


def gathered_blocks(block, axis):
    from_below = passed_along(block, "y", 1)
    from_above = passed_along(block, "y", -1)
    far_low = passed_along(jnp.split(from_below, 2, axis=axis)[0], "y", 1)
    far_high = passed_along(jnp.split(from_above, 2, axis=axis)[1], "y", -1)
    return [block, from_below, from_above], [far_low, far_high]


def body(acts, norm_gain, router, routes, w_gate, w_up, w_down):
    experts_here = router.shape[2]
    row_size = lax.axis_size("z") * lax.axis_size("core")
    tok_local = acts.shape[2]
    width = acts.shape[3]
    capacity = 2 * tok_local // experts_here
    gain_row = norm_gain[0]
    router_mat = router[0]
    gate_near, gate_far = gathered_blocks(w_gate[0, 0], 1)
    up_near, up_far = gathered_blocks(w_up[0, 0], 1)
    down_near, down_far = gathered_blocks(w_down[0, 0], 0)
    near_hid = sum(mat.shape[1] for mat in gate_near)
    far_hid = sum(mat.shape[1] for mat in gate_far)
    near_gate_up = jnp.concatenate(gate_near + up_near, axis=1)
    near_down = jnp.concatenate(down_near, axis=0)
    far_gate_up = jnp.concatenate(gate_far + up_far, axis=1)
    far_down = jnp.concatenate(down_far, axis=0)

    def expert_part(rows_in, gate_up, down_all, hid):
        both = jnp.dot(rows_in, gate_up, preferred_element_type=jnp.float32)
        hidden = (jax.nn.silu(both[:, :hid]) * both[:, hid:]).astype(jnp.bfloat16)
        return jnp.dot(hidden, down_all, preferred_element_type=jnp.float32)

    def expert_compute(rows_in):
        near = expert_part(rows_in, near_gate_up, near_down, near_hid)
        far = expert_part(rows_in, far_gate_up, far_down, far_hid)
        return (near + far).astype(jnp.bfloat16)

    def prepare(tokens_in, route_ids):
        x_float = tokens_in.astype(jnp.float32)
        mean_sq = jnp.mean(x_float * x_float, axis=1, keepdims=True)
        normed = (x_float * lax.rsqrt(mean_sq + 1e-06) * gain_row[None, :]).astype(jnp.bfloat16)
        scores = jnp.dot(normed, router_mat, preferred_element_type=jnp.float32)
        chosen = route_ids[:, 0]
        onehot = (chosen[:, None] == jnp.arange(experts_here, dtype=jnp.int32)[None, :]).astype(
            jnp.int32
        )
        gate_val = jax.nn.sigmoid(jnp.sum(scores * onehot.astype(jnp.float32), axis=1))
        slot_of = jnp.sum(jnp.cumsum(onehot, axis=0) * onehot, axis=1) - 1
        flat_slot = chosen * capacity + slot_of
        placing = (
            flat_slot[None, :] == jnp.arange(experts_here * capacity, dtype=jnp.int32)[:, None]
        ).astype(jnp.bfloat16)
        outbox = jnp.dot(placing, normed, preferred_element_type=jnp.float32).astype(jnp.bfloat16)
        return x_float, gate_val, placing, outbox.reshape(row_size, capacity, width)

    def returned(summed):
        back = lax.all_to_all(
            summed.reshape(row_size, capacity, width), ROW, split_axis=0, concat_axis=0, tiled=True
        )
        return back.reshape(experts_here * capacity, width)

    def finish(arrived, x_float, gate_val, placing, split_return):
        rows_in = arrived.reshape(-1, width)
        if split_return:
            near = expert_part(rows_in, near_gate_up, near_down, near_hid).astype(jnp.bfloat16)
            far = expert_part(rows_in, far_gate_up, far_down, far_hid).astype(jnp.bfloat16)
            back = returned(near).astype(jnp.float32) + returned(far).astype(jnp.float32)
        else:
            back = returned(expert_compute(rows_in))
        picked = jnp.dot(placing.T, back, preferred_element_type=jnp.float32)
        return (x_float + gate_val[:, None] * picked).astype(jnp.bfloat16)

    micro_count = acts.shape[1]
    carried = [acts[0, micro_idx] for micro_idx in range(micro_count)]
    for round_idx in range(routes.shape[1]):
        ready = [prepare(carried[m], routes[0, round_idx, m]) for m in range(micro_count)]
        if round_idx == 0:
            stacked = jnp.stack([parts[3] for parts in ready], axis=1)
            together = lax.all_to_all(stacked, ROW, split_axis=0, concat_axis=0, tiled=True)
            arrivals = [together[:, m] for m in range(micro_count)]
        else:
            arrivals = [
                lax.all_to_all(parts[3], ROW, split_axis=0, concat_axis=0, tiled=True)
                for parts in ready
            ]
        carried = [
            passed_along(finish(arrivals[m], *ready[m][:3], round_idx == 0), "section", 1)
            for m in range(micro_count)
        ]
    return jnp.stack(carried)[None]


def solution(mesh):
    n_sec, n_exp = mesh.devices.shape
    n_core = 2
    n_y = n_exp // (n_core * 8)
    grid = mesh.devices.reshape(n_sec, n_y, n_exp // (n_y * n_core), n_core)
    fine = Mesh(grid, ("section", "y", "z", "core"))
    in_specs = (
        P("section", None, EXP, None),
        P("section", None),
        P("section", None, None),
        P("section", None, None, EXP, None),
        P("section", EXP, None, None),
        P("section", EXP, None, None),
        P("section", EXP, None, None),
    )
    out_specs = P("section", None, EXP, None)
    return jax.shard_map(body, mesh=fine, in_specs=in_specs, out_specs=out_specs, check_vma=False)
```
